512 devices in a mesh: team: 128 (over x_lo, y, z), rep: 4 (over x_hi, core).
Axes of the slice: x: 4 (x_hi: 2, x_lo: 2; x = x_hi * 2 + x_lo), y: 4, z: 16, core: 2. Of those that a mesh axis runs over, the one named last changes fastest.
Arguments:
- features: bfloat16 [131072, 128], P('team'), may hold values from -6 to 6
- weight: bfloat16 [128, 128], replicated, may hold values from -0.5 to 0.5
- out_grad: bfloat16 [131072, 128], P(('team', 'rep')), may hold values from -6 to 6
- tiles: bfloat16 [1024, 5, 8, 128, 128], P(('team', 'rep')), may hold values from -0.125 to 0.125
- coords: int32 [1024, 5, 8], P(('team', 'rep')), may hold values from 0 to 7, as said below
- counts: int32 [1024, 5], P(('team', 'rep')), may hold values from 1 to 8, as said below
Outputs:
- activated: bfloat16 [131072, 128], P(('team', 'rep'))
- grad_weight: float32 [128, 128], replicated
- grad_features: bfloat16 [131072, 128], P(('team', 'rep'))
The draws below stay inside these ranges and needn't reach their ends.
Inputs may be any that keep to these rules, and one draw needn't show every extreme that they name: `coords`: the live and dead slots of one panel and section name distinct column tiles. `counts`: in every draw all panels of some team have 8 live slots for every section.
All inputs are finite; a program needn't handle non-finite values.
Results may differ from the reference program's by a relative error of at most 0.013.
Values may be sent and summed in bfloat16 or wider, within the bound.
No kernel may reach another device: no remote copies, remote signals or barrier semaphores. Data moves between devices by JAX's collectives and lax.ppermute only.
A program may use at most 64 MiB of HBM per device.

```python
import math
import jax
import jax.numpy as jnp

F = 128
TILE = 128
SECTIONS = 5
TEAM_PANELS = 8
SLOTS = 8
PANELS = 1024
NODES = 131072
N_TEAM = 128


def draw_coords(key, part):
    keys = jax.random.split(key, PANELS * SECTIONS)

    def one_order(single_key):
        return jax.random.permutation(single_key, TEAM_PANELS)
    orders = jax.vmap(one_order)(keys)
    return orders[:, :SLOTS].reshape(PANELS, SECTIONS, SLOTS).astype(jnp.int32)


def draw_counts(key, part):
    first_key, second_key, third_key = jax.random.split(key, 3)
    team_count = PANELS // TEAM_PANELS
    team_extra = jax.random.randint(first_key, (team_count,), 0, SLOTS // 2 + 1)
    base_count = jax.random.randint(second_key, (PANELS, SECTIONS), 1, SLOTS // 2 + 1)
    team_of = jnp.arange(PANELS, dtype=jnp.int32) // TEAM_PANELS
    raised = base_count + team_extra[team_of][:, None]
    full_team = jax.random.randint(third_key, (), 0, team_count)
    raised = jnp.where((team_of == full_team)[:, None], SLOTS, raised)
    return jnp.minimum(raised, SLOTS).astype(jnp.int32)


def level_of(own_key, dims, pieces, smallest, largest):
    loudness, own = 1.0, jax.random.fold_in(own_key, 6)
    for position, blocks in pieces:
        steps = jnp.exp(jax.random.uniform(jax.random.fold_in(own, position), (blocks,), jnp.float32, smallest / len(pieces), largest / len(pieces)))
        loudness = loudness * jnp.repeat(steps, dims[position] // blocks).reshape([-1 if axis == position else 1 for axis in range(len(dims))])
    return loudness


def noise(own_key, dims, scale, bound, cuts=(), kind=jnp.bfloat16):
    drawn = jax.random.normal(own_key, dims, jnp.float32) * scale
    if len(cuts) > 0:
        drawn = level_of(own_key, dims, cuts, -0.22, 0.18) * drawn
    return jnp.clip(drawn, min=-bound, max=bound).astype(kind)


def setup_inputs(seed: int = 0) -> dict:
    streams_of = jax.random.split(jax.random.key(seed), 7)
    return {
        "features": noise(streams_of[0], (NODES, F), 1.0, 6.0, ((0, 128),)),
        "weight": noise(streams_of[1], (F, F), F ** -0.5, 0.5),
        "out_grad": noise(streams_of[2], (NODES, F), 1.0, 6.0, ((0, 512),)),
        "tiles": noise(streams_of[3], (PANELS, SECTIONS, SLOTS, TILE, TILE), (TILE * SLOTS * SECTIONS // 2) ** -0.5, 0.125, ((0, 512),)),
        "coords": draw_coords(jax.random.fold_in(streams_of[6], 71), 0),
        "counts": draw_counts(jax.random.fold_in(streams_of[6], 71), 0),
    }


def reference(features, weight, out_grad, tiles, coords, counts):
    panel_count, section_count, slot_count, tile_size, _ = tiles.shape
    feature_width = features.shape[1]
    reach_size = (section_count - 1) // 2
    feature_tiles = features.reshape(-1, tile_size, feature_width)
    team_of = (jnp.arange(panel_count, dtype=jnp.int32) // TEAM_PANELS).astype(jnp.int32)
    live_slots = jnp.arange(slot_count, dtype=jnp.int32)[None, None, :] < counts[:, :, None]
    running = jnp.zeros((panel_count, tile_size, feature_width), jnp.float32)
    for section_index in range(section_count):
        source_team = (team_of + section_index - reach_size) % N_TEAM
        for slot_index in range(slot_count):
            column_tile = (source_team * TEAM_PANELS + coords[:, section_index, slot_index]).astype(jnp.int32)
            current = jnp.where(live_slots[:, section_index, slot_index][:, None, None], tiles[:, section_index, slot_index], jnp.zeros_like(tiles[:, 0, 0])).astype(jnp.float32)
            picked = feature_tiles[column_tile].astype(jnp.float32)
            running = running + jnp.einsum('pab,pbf->paf', current, picked)
    aggregated = running.reshape(-1, feature_width).astype(jnp.bfloat16)
    pre_act = jnp.dot(aggregated, weight, preferred_element_type=jnp.float32)
    sigmoid_value = jax.nn.sigmoid(pre_act)
    activated = (pre_act * sigmoid_value).astype(jnp.bfloat16)
    gate_grad = (out_grad.astype(jnp.float32) * sigmoid_value * (1.0 + pre_act * (1.0 - sigmoid_value))).astype(jnp.bfloat16)
    grad_weight = jnp.dot(aggregated.T, gate_grad, preferred_element_type=jnp.float32) * (1.0 / math.sqrt(NODES))
    back_rows = jnp.dot(gate_grad, weight.T, preferred_element_type=jnp.float32).astype(jnp.bfloat16)
    back_tiles = back_rows.reshape(panel_count, tile_size, feature_width).astype(jnp.float32)
    gradient_sum = jnp.zeros((panel_count, tile_size, feature_width), jnp.float32)
    for section_index in range(section_count):
        source_team = (team_of + section_index - reach_size) % N_TEAM
        for slot_index in range(slot_count):
            column_tile = (source_team * TEAM_PANELS + coords[:, section_index, slot_index]).astype(jnp.int32)
            current = jnp.where(live_slots[:, section_index, slot_index][:, None, None], tiles[:, section_index, slot_index], jnp.zeros_like(tiles[:, 0, 0])).astype(jnp.float32)
            contrib = jnp.einsum('pab,paf->pbf', current, back_tiles)
            gradient_sum = gradient_sum.at[column_tile].add(contrib)
    grad_features = gradient_sum.reshape(-1, feature_width).astype(jnp.bfloat16)
    return (activated, grad_weight, grad_features)
```

```python
import math

import jax
import jax.numpy as jnp
from jax import lax
from jax.sharding import PartitionSpec as P


def from_behind(block, axis, distance):
    devices = range(lax.axis_size(axis))
    route = [((i - distance) % len(devices), i) for i in devices]
    return lax.ppermute(block, axis, route)


def butterfly_sum(block, axes):
    for axis in axes:
        size = lax.axis_size(axis)
        if size & (size - 1):
            block = lax.psum(block, axis)
            continue
        distance = 1
        while distance < size:
            route = [(i, i ^ distance) for i in range(size)]
            block = block + lax.ppermute(block, axis, route)
            distance *= 2
    return block


def neighbour_blocks(features, reach_size):
    blocks = {0: features}
    ahead_block = features
    behind_block = features
    for offset in range(1, reach_size + 1):
        ahead_block = from_behind(ahead_block, "team", -1)
        behind_block = from_behind(behind_block, "team", 1)
        blocks[offset] = ahead_block
        blocks[-offset] = behind_block
    return blocks


def deliver(pieces, reach_size):
    combined = pieces[0]
    upward = pieces[reach_size]
    downward = pieces[-reach_size]
    for step_index in range(reach_size):
        upward = from_behind(upward.astype(jnp.bfloat16), "team", 1).astype(upward.dtype)
        downward = from_behind(downward.astype(jnp.bfloat16), "team", -1).astype(downward.dtype)
        if step_index < reach_size - 1:
            upward = upward + pieces[reach_size - 1 - step_index]
            downward = downward + pieces[-(reach_size - 1 - step_index)]
    combined = combined + upward + downward
    return combined


def aggregate(running, source_tiles, section_tiles, section_coords, section_live, slot_bound):

    def aggregate_add_slot(slot_index, partial_rows):
        column_tile = lax.dynamic_index_in_dim(section_coords, slot_index, 1, keepdims=False)
        picked = jnp.take(source_tiles, column_tile, axis=0)
        current = lax.dynamic_index_in_dim(section_tiles, slot_index, 1, keepdims=False)
        keep_mask = lax.dynamic_index_in_dim(section_live, slot_index, 1, keepdims=False)
        current = jnp.where(keep_mask[:, None, None], current, jnp.zeros_like(current))
        return partial_rows + jnp.einsum(
            "pab,pbf->paf", current, picked, preferred_element_type=jnp.float32
        )

    return lax.fori_loop(0, slot_bound, aggregate_add_slot, running)


def spread(back_tiles, section_tiles, section_coords, section_live, slot_bound, column_count):
    panel_dev, _, tile_size, _ = section_tiles.shape
    feature_width = back_tiles.shape[2]

    def spread_add_slot(slot_index, partial_sums):
        column_tile = lax.dynamic_index_in_dim(section_coords, slot_index, 1, keepdims=False)
        current = lax.dynamic_index_in_dim(section_tiles, slot_index, 1, keepdims=False)
        keep_mask = lax.dynamic_index_in_dim(section_live, slot_index, 1, keepdims=False)
        current = jnp.where(keep_mask[:, None, None], current, jnp.zeros_like(current))
        contrib = jnp.einsum(
            "pab,paf->pbf", current, back_tiles, preferred_element_type=jnp.float32
        )
        return partial_sums.at[column_tile].add(contrib)

    initial = jnp.zeros((column_count, tile_size, feature_width), jnp.float32)
    return lax.fori_loop(0, slot_bound, spread_add_slot, initial)


def body(features, weight, out_grad, tiles, coords, counts):
    panel_dev, section_count, slot_count, tile_size, _ = tiles.shape
    team_rows, feature_width = features.shape
    column_count = team_rows // tile_size
    reach_size = (section_count - 1) // 2
    nodes_total = team_rows * lax.axis_size("team")
    live_slots = lax.broadcasted_iota(jnp.int32, coords.shape, 2) < counts[:, :, None]
    slot_bounds = jnp.max(counts, axis=0)
    blocks = neighbour_blocks(features, reach_size)
    running = jnp.zeros((panel_dev, tile_size, feature_width), jnp.float32)
    for section_index in range(section_count):
        source_tiles = blocks[section_index - reach_size].reshape(
            column_count, tile_size, feature_width
        )
        running = aggregate(
            running,
            source_tiles,
            tiles[:, section_index],
            coords[:, section_index],
            live_slots[:, section_index],
            slot_bounds[section_index],
        )
    aggregated = running.reshape(-1, feature_width).astype(jnp.bfloat16)
    pre_act = jnp.dot(aggregated, weight, preferred_element_type=jnp.float32)
    sigmoid_value = jax.nn.sigmoid(pre_act)
    activated = (pre_act * sigmoid_value).astype(jnp.bfloat16)
    gate_grad = (
        out_grad.astype(jnp.float32) * sigmoid_value * (1.0 + pre_act * (1.0 - sigmoid_value))
    ).astype(jnp.bfloat16)
    local_weight_grad = lax.dot_general(
        aggregated, gate_grad, (((0,), (0,)), ((), ())), preferred_element_type=jnp.float32
    )
    grad_weight = butterfly_sum(local_weight_grad, ("rep", "team")) * (1.0 / math.sqrt(nodes_total))
    back_rows = lax.dot_general(
        gate_grad, weight, (((1,), (1,)), ((), ())), preferred_element_type=jnp.float32
    ).astype(jnp.bfloat16)
    back_tiles = back_rows.reshape(panel_dev, tile_size, feature_width)
    partial_list = []
    for section_index in range(section_count):
        section_sums = spread(
            back_tiles,
            tiles[:, section_index],
            coords[:, section_index],
            live_slots[:, section_index],
            slot_bounds[section_index],
            column_count,
        )
        partial_list.append(section_sums.reshape(team_rows, feature_width))
    pieces = {}
    for section_index in range(section_count):
        pieces[section_index - reach_size] = partial_list[section_index]
    team_total = deliver(pieces, reach_size)
    gradient_share = lax.psum_scatter(
        team_total.astype(jnp.bfloat16), "rep", scatter_dimension=0, tiled=True
    )
    return (activated, grad_weight, gradient_share)


def solution(mesh):
    placed = (
        P("team", None),
        P(),
        P(("team", "rep"), None),
        P(("team", "rep"), None, None, None, None),
        P(("team", "rep"), None, None),
        P(("team", "rep"), None),
    )
    return jax.shard_map(
        body,
        mesh=mesh,
        in_specs=placed,
        out_specs=(P(("team", "rep"), None), P(), P(("team", "rep"), None)),
        check_vma=False,
    )
```

```python
import functools
import math

import jax
import jax.numpy as jnp
from jax import lax
from jax.experimental import pallas as pl
from jax.experimental.pallas import tpu as pltpu
from jax.sharding import PartitionSpec as P


def from_behind(block, axis, distance):
    devices = range(lax.axis_size(axis))
    route = [((i - distance) % len(devices), i) for i in devices]
    return lax.ppermute(block, axis, route)


def butterfly_sum(block, axes):
    for axis in axes:
        size = lax.axis_size(axis)
        if size & (size - 1):
            block = lax.psum(block, axis)
            continue
        distance = 1
        while distance < size:
            route = [(i, i ^ distance) for i in range(size)]
            block = block + lax.ppermute(block, axis, route)
            distance *= 2
    return block


def neighbour_blocks(features, reach_size):
    blocks = {0: features}
    ahead_block = features
    behind_block = features
    for offset in range(1, reach_size + 1):
        ahead_block = from_behind(ahead_block, "team", -1)
        behind_block = from_behind(behind_block, "team", 1)
        blocks[offset] = ahead_block
        blocks[-offset] = behind_block
    return blocks


def layer_kernel(coords_ref, counts_ref, *refs, section_count, slot_count, panel_dev, tile_size):
    feature_refs = refs[:section_count]
    tiles_ref, out_grad_ref, weight_ref, act_ref, wgrad_ref, sums_ref = refs[section_count:]
    weight = weight_ref[...]
    column_count = feature_refs[0].shape[0] // tile_size
    direct_first = slot_count == column_count

    def slot_entry(g, s, k):
        base = (g * section_count + s) * slot_count + k
        column = jnp.clip(coords_ref[base], 0, column_count - 1)
        live = k < counts_ref[g * section_count + s]
        return column, live

    aggregated_rows = []
    gate_rows = []
    for g in range(panel_dev):
        total = jnp.zeros((tile_size, weight.shape[1]), jnp.float32)
        for s in range(section_count):
            for k in range(slot_count):
                column, live = slot_entry(g, s, k)
                start = pl.multiple_of(column * tile_size, tile_size)
                picked = feature_refs[s][pl.ds(start, tile_size), :]
                product = jnp.dot(tiles_ref[g, s, k], picked, preferred_element_type=jnp.float32)
                total = total + jnp.where(live, product, 0.0)
        aggregated = total.astype(jnp.bfloat16)
        pre_act = jnp.dot(aggregated, weight, preferred_element_type=jnp.float32)
        sigmoid_value = jax.nn.sigmoid(pre_act)
        rows = pl.ds(g * tile_size, tile_size)
        act_ref[rows, :] = (pre_act * sigmoid_value).astype(act_ref.dtype)
        out_grad = out_grad_ref[rows, :].astype(jnp.float32)
        gate = (out_grad * sigmoid_value * (1.0 + pre_act * (1.0 - sigmoid_value))).astype(jnp.bfloat16)
        aggregated_rows.append(aggregated)
        gate_rows.append(gate)

    aggregated_all = jnp.concatenate(aggregated_rows, axis=0)
    gate_all = jnp.concatenate(gate_rows, axis=0)
    wgrad_ref[...] = lax.dot_general(
        aggregated_all, gate_all, (((0,), (0,)), ((), ())), preferred_element_type=jnp.float32
    )
    if not direct_first:
        sums_ref[...] = jnp.zeros(sums_ref.shape, sums_ref.dtype)
    for g in range(panel_dev):
        back = lax.dot_general(
            gate_rows[g], weight, (((1,), (1,)), ((), ())), preferred_element_type=jnp.float32
        ).astype(jnp.bfloat16)
        for s in range(section_count):
            for k in range(slot_count):
                column, live = slot_entry(g, s, k)
                start = pl.multiple_of(column * tile_size, tile_size)
                contrib = lax.dot_general(
                    tiles_ref[g, s, k], back, (((0,), (0,)), ((), ())),
                    preferred_element_type=jnp.float32,
                )
                contrib = jnp.where(live, contrib, 0.0)
                if g == 0 and direct_first:
                    sums_ref[s, pl.ds(start, tile_size), :] = contrib
                else:
                    sums_ref[s, pl.ds(start, tile_size), :] += contrib


def layer_call(source_blocks, tiles, out_grad, weight, coords, counts):
    panel_dev, section_count, slot_count, tile_size, _ = tiles.shape
    team_rows, feature_width = source_blocks[0].shape
    kernel = functools.partial(
        layer_kernel,
        section_count=section_count,
        slot_count=slot_count,
        panel_dev=panel_dev,
        tile_size=tile_size,
    )
    smem = pl.BlockSpec(memory_space=pltpu.SMEM)
    vmem = pl.BlockSpec(memory_space=pltpu.VMEM)
    matmuls = 2 * panel_dev * section_count * slot_count + 4 * panel_dev
    return pl.pallas_call(
        kernel,
        out_shape=(
            jax.ShapeDtypeStruct(out_grad.shape, jnp.bfloat16),
            jax.ShapeDtypeStruct((feature_width, feature_width), jnp.float32),
            jax.ShapeDtypeStruct((section_count, team_rows, feature_width), jnp.float32),
        ),
        in_specs=[smem, smem] + [vmem] * (section_count + 3),
        out_specs=(vmem, vmem, vmem),
        compiler_params=pltpu.CompilerParams(vmem_limit_bytes=48 * 1024 * 1024),
        cost_estimate=pl.CostEstimate(
            flops=2 * matmuls * tile_size * tile_size * feature_width,
            transcendentals=panel_dev * tile_size * feature_width,
            bytes_accessed=tiles.size * 2 + section_count * team_rows * feature_width * 6,
        ),
    )(coords.reshape(-1), counts.reshape(-1), *source_blocks, tiles, out_grad, weight)


def split_pick(block, index, axis):
    kept = lax.dynamic_index_in_dim(block, index, axis, keepdims=False)
    sent = lax.dynamic_index_in_dim(block, 1 - index, axis, keepdims=False)
    return kept, sent


def swap_with(block, axis, mask):
    size = lax.axis_size(axis)
    route = [(i, i ^ mask) for i in range(size)]
    return lax.ppermute(block, axis, route)


def body(features, weight, out_grad, tiles, coords, counts):
    panel_dev, section_count, slot_count, tile_size, _ = tiles.shape
    team_rows, feature_width = features.shape
    reach_size = (section_count - 1) // 2
    nodes_total = team_rows * lax.axis_size("team")
    rep_size = lax.axis_size("rep")
    blocks = neighbour_blocks(features, reach_size)
    source_blocks = [blocks[s - reach_size] for s in range(section_count)]
    activated, local_weight_grad, sums = layer_call(
        source_blocks, tiles, out_grad, weight, coords, counts
    )
    grad_weight = butterfly_sum(local_weight_grad, ("rep", "team")) * (1.0 / math.sqrt(nodes_total))

    rep_index = lax.axis_index("rep")
    if rep_size == 4:
        quarter = team_rows // 4
        staged = sums.reshape(section_count, 2, 2, quarter, feature_width)
        kept, sent = split_pick(staged, rep_index % 2, 2)
        kept = kept + swap_with(sent.astype(jnp.bfloat16), "rep", 1).astype(jnp.float32)
        kept, sent = split_pick(kept, rep_index // 2, 1)
        share = kept + swap_with(sent.astype(jnp.bfloat16), "rep", 2).astype(jnp.float32)
    else:
        share = lax.psum_scatter(sums, "rep", scatter_dimension=1, tiled=True)

    total = share[reach_size]
    for s in range(section_count):
        if s == reach_size:
            continue
        shift = s - reach_size
        arrived = from_behind(share[s].astype(jnp.bfloat16), "team", shift)
        total = total + arrived.astype(jnp.float32)
    gradient_share = total.astype(jnp.bfloat16)
    return (activated, grad_weight, gradient_share)


def solution(mesh):
    placed = (
        P("team", None),
        P(),
        P(("team", "rep"), None),
        P(("team", "rep"), None, None, None, None),
        P(("team", "rep"), None, None),
        P(("team", "rep"), None),
    )
    return jax.shard_map(
        body,
        mesh=mesh,
        in_specs=placed,
        out_specs=(P(("team", "rep"), None), P(), P(("team", "rep"), None)),
        check_vma=False,
    )
```

```python
import functools
import math

import jax
import jax.numpy as jnp
from jax import lax
from jax.experimental import pallas as pl
from jax.experimental.pallas import tpu as pltpu
from jax.sharding import PartitionSpec as P


def from_behind(block, axis, distance):
    devices = range(lax.axis_size(axis))
    route = [((i - distance) % len(devices), i) for i in devices]
    return lax.ppermute(block, axis, route)


def butterfly_sum(block, axes):
    for axis in axes:
        size = lax.axis_size(axis)
        if size & (size - 1):
            block = lax.psum(block, axis)
            continue
        distance = 1
        while distance < size:
            route = [(i, i ^ distance) for i in range(size)]
            block = block + lax.ppermute(block, axis, route)
            distance *= 2
    return block


def neighbour_blocks(features, reach_size):
    blocks = {0: features}
    ahead_block = features
    behind_block = features
    for offset in range(1, reach_size + 1):
        ahead_block = from_behind(ahead_block, "team", -1)
        behind_block = from_behind(behind_block, "team", 1)
        blocks[offset] = ahead_block
        blocks[-offset] = behind_block
    return blocks


def layer_kernel(coords_ref, counts_ref, *refs, section_count, slot_count, panel_dev, tile_size):
    feature_refs = refs[:section_count]
    tiles_ref, out_grad_ref, weight_ref, act_ref, wgrad_ref, sums_ref = refs[section_count:]
    weight = weight_ref[...]
    column_count = feature_refs[0].shape[0] // tile_size
    direct_first = slot_count == column_count

    def slot_entry(g, s, k):
        base = (g * section_count + s) * slot_count + k
        column = jnp.clip(coords_ref[base], 0, column_count - 1)
        live = k < counts_ref[g * section_count + s]
        return column, live

    aggregated_rows = []
    gate_rows = []
    for g in range(panel_dev):
        total = jnp.zeros((tile_size, weight.shape[1]), jnp.float32)
        for s in range(section_count):
            for k in range(slot_count):
                column, live = slot_entry(g, s, k)
                start = pl.multiple_of(column * tile_size, tile_size)
                picked = feature_refs[s][pl.ds(start, tile_size), :]
                product = jnp.dot(tiles_ref[g, s, k], picked, preferred_element_type=jnp.float32)
                total = total + jnp.where(live, product, 0.0)
        aggregated = total.astype(jnp.bfloat16)
        pre_act = jnp.dot(aggregated, weight, preferred_element_type=jnp.float32)
        sigmoid_value = jax.nn.sigmoid(pre_act)
        rows = pl.ds(g * tile_size, tile_size)
        act_ref[rows, :] = (pre_act * sigmoid_value).astype(act_ref.dtype)
        out_grad = out_grad_ref[rows, :].astype(jnp.float32)
        gate = (out_grad * sigmoid_value * (1.0 + pre_act * (1.0 - sigmoid_value))).astype(jnp.bfloat16)
        aggregated_rows.append(aggregated)
        gate_rows.append(gate)

    aggregated_all = jnp.concatenate(aggregated_rows, axis=0)
    gate_all = jnp.concatenate(gate_rows, axis=0)
    wgrad_ref[...] = lax.dot_general(
        aggregated_all, gate_all, (((0,), (0,)), ((), ())), preferred_element_type=jnp.float32
    )
    if not direct_first:
        sums_ref[...] = jnp.zeros(sums_ref.shape, sums_ref.dtype)
    for g in range(panel_dev):
        back = lax.dot_general(
            gate_rows[g], weight, (((1,), (1,)), ((), ())), preferred_element_type=jnp.float32
        ).astype(jnp.bfloat16)
        for s in range(section_count):
            for k in range(slot_count):
                column, live = slot_entry(g, s, k)
                start = pl.multiple_of(column * tile_size, tile_size)
                contrib = lax.dot_general(
                    tiles_ref[g, s, k], back, (((0,), (0,)), ((), ())),
                    preferred_element_type=jnp.float32,
                )
                contrib = jnp.where(live, contrib, 0.0)
                if g == 0 and direct_first:
                    sums_ref[s, pl.ds(start, tile_size), :] = contrib
                else:
                    sums_ref[s, pl.ds(start, tile_size), :] += contrib


def layer_call(source_blocks, tiles, out_grad, weight, coords, counts):
    panel_dev, section_count, slot_count, tile_size, _ = tiles.shape
    team_rows, feature_width = source_blocks[0].shape
    kernel = functools.partial(
        layer_kernel,
        section_count=section_count,
        slot_count=slot_count,
        panel_dev=panel_dev,
        tile_size=tile_size,
    )
    smem = pl.BlockSpec(memory_space=pltpu.SMEM)
    vmem = pl.BlockSpec(memory_space=pltpu.VMEM)
    matmuls = 2 * panel_dev * section_count * slot_count + 4 * panel_dev
    return pl.pallas_call(
        kernel,
        out_shape=(
            jax.ShapeDtypeStruct(out_grad.shape, jnp.bfloat16),
            jax.ShapeDtypeStruct((feature_width, feature_width), jnp.float32),
            jax.ShapeDtypeStruct((section_count, team_rows, feature_width), jnp.float32),
        ),
        in_specs=[smem, smem] + [vmem] * (section_count + 3),
        out_specs=(vmem, vmem, vmem),
        compiler_params=pltpu.CompilerParams(vmem_limit_bytes=48 * 1024 * 1024),
        cost_estimate=pl.CostEstimate(
            flops=2 * matmuls * tile_size * tile_size * feature_width,
            transcendentals=panel_dev * tile_size * feature_width,
            bytes_accessed=tiles.size * 2 + section_count * team_rows * feature_width * 6,
        ),
    )(coords.reshape(-1), counts.reshape(-1), *source_blocks, tiles, out_grad, weight)


def swap_with(block, axis, mask):
    size = lax.axis_size(axis)
    route = [(i, i ^ mask) for i in range(size)]
    return lax.ppermute(block, axis, route)


def team_total_sum(block):
    size = lax.axis_size("team")
    rows = block.shape[0]
    if rows % size:
        return butterfly_sum(block, ("team",))
    pieces = lax.all_to_all(block.reshape(size, rows // size, -1), "team", 0, 0, tiled=True)
    own = jnp.sum(pieces, axis=0)
    copies = jnp.broadcast_to(own[None], (size,) + own.shape)
    return lax.all_to_all(copies, "team", 0, 0, tiled=True).reshape(block.shape)


def body(features, weight, out_grad, tiles, coords, counts):
    panel_dev, section_count, slot_count, tile_size, _ = tiles.shape
    team_rows, feature_width = features.shape
    reach_size = (section_count - 1) // 2
    nodes_total = team_rows * lax.axis_size("team")
    rep_size = lax.axis_size("rep")
    source_blocks = [
        features if s == reach_size else from_behind(features, "team", reach_size - s)
        for s in range(section_count)
    ]
    activated, local_weight_grad, sums = layer_call(
        source_blocks, tiles, out_grad, weight, coords, counts
    )
    if rep_size != 4:
        grad_weight = butterfly_sum(local_weight_grad, ("rep", "team"))
        share = lax.psum_scatter(sums, "rep", scatter_dimension=1, tiled=True)
        total = share[reach_size]
        for s in range(section_count):
            if s != reach_size:
                arrived = from_behind(share[s].astype(jnp.bfloat16), "team", s - reach_size)
                total = total + arrived.astype(jnp.float32)
        return (activated, grad_weight * (1.0 / math.sqrt(nodes_total)), total.astype(jnp.bfloat16))

    rep_index = lax.axis_index("rep")
    core_bit = rep_index % 2
    chip_bit = rep_index // 2
    quarter = team_rows // 4
    half_rows = 2 * quarter
    staged = sums.reshape(section_count, 2, 2, quarter, feature_width)
    kept = lax.dynamic_index_in_dim(staged, core_bit, 2, keepdims=False)
    sent = lax.dynamic_index_in_dim(staged, 1 - core_bit, 2, keepdims=False)
    packet = jnp.concatenate(
        [sent.reshape(section_count * half_rows, feature_width), local_weight_grad], axis=0
    )
    arrived = swap_with(packet, "rep", 1)
    kept = kept.reshape(section_count, half_rows, feature_width) + arrived[
        : section_count * half_rows
    ].reshape(section_count, half_rows, feature_width)
    weight_grad = local_weight_grad + arrived[section_count * half_rows :]

    total = kept[reach_size]
    for s in range(section_count):
        if s != reach_size:
            moved = from_behind(kept[s].astype(jnp.bfloat16), "team", s - reach_size)
            total = total + moved.astype(jnp.float32)

    staged = total.reshape(2, quarter, feature_width)
    kept = lax.dynamic_index_in_dim(staged, chip_bit, 0, keepdims=False)
    sent = lax.dynamic_index_in_dim(staged, 1 - chip_bit, 0, keepdims=False)
    arrived = swap_with(jnp.concatenate([sent, weight_grad], axis=0), "rep", 2)
    gradient_share = (kept + arrived[:quarter]).astype(jnp.bfloat16)
    weight_grad = weight_grad + arrived[quarter:]
    grad_weight = team_total_sum(weight_grad) * (1.0 / math.sqrt(nodes_total))
    return (activated, grad_weight, gradient_share)


def solution(mesh):
    placed = (
        P("team", None),
        P(),
        P(("team", "rep"), None),
        P(("team", "rep"), None, None, None, None),
        P(("team", "rep"), None, None),
        P(("team", "rep"), None),
    )
    return jax.shard_map(
        body,
        mesh=mesh,
        in_specs=placed,
        out_specs=(P(("team", "rep"), None), P(), P(("team", "rep"), None)),
        check_vma=False,
    )
```

```python
import functools
import math

import jax
import jax.numpy as jnp
from jax import lax
from jax.experimental import pallas as pl
from jax.experimental.pallas import tpu as pltpu
from jax.sharding import PartitionSpec as P


def from_behind(block, axis, distance):
    devices = range(lax.axis_size(axis))
    route = [((i - distance) % len(devices), i) for i in devices]
    return lax.ppermute(block, axis, route)


def butterfly_sum(block, axes):
    for axis in axes:
        size = lax.axis_size(axis)
        if size & (size - 1):
            block = lax.psum(block, axis)
            continue
        distance = 1
        while distance < size:
            route = [(i, i ^ distance) for i in range(size)]
            block = block + lax.ppermute(block, axis, route)
            distance *= 2
    return block


def neighbour_blocks(features, reach_size):
    blocks = {0: features}
    ahead_block = features
    behind_block = features
    for offset in range(1, reach_size + 1):
        ahead_block = from_behind(ahead_block, "team", -1)
        behind_block = from_behind(behind_block, "team", 1)
        blocks[offset] = ahead_block
        blocks[-offset] = behind_block
    return blocks


def layer_kernel(coords_ref, counts_ref, *refs, section_count, slot_count, panel_dev, tile_size):
    feature_refs = refs[:section_count]
    tiles_ref, out_grad_ref, weight_ref, act_ref, wgrad_ref, sums_ref = refs[section_count:]
    weight = weight_ref[...]
    column_count = feature_refs[0].shape[0] // tile_size
    direct_first = slot_count == column_count

    def slot_entry(g, s, k):
        base = (g * section_count + s) * slot_count + k
        column = jnp.clip(coords_ref[base], 0, column_count - 1)
        live = k < counts_ref[g * section_count + s]
        return column, live

    aggregated_rows = []
    gate_rows = []
    for g in range(panel_dev):
        total = jnp.zeros((tile_size, weight.shape[1]), jnp.float32)
        for s in range(section_count):
            for k in range(slot_count):
                column, live = slot_entry(g, s, k)
                start = pl.multiple_of(column * tile_size, tile_size)
                picked = feature_refs[s][pl.ds(start, tile_size), :]
                product = jnp.dot(tiles_ref[g, s, k], picked, preferred_element_type=jnp.float32)
                total = total + jnp.where(live, product, 0.0)
        aggregated = total.astype(jnp.bfloat16)
        pre_act = jnp.dot(aggregated, weight, preferred_element_type=jnp.float32)
        sigmoid_value = jax.nn.sigmoid(pre_act)
        rows = pl.ds(g * tile_size, tile_size)
        act_ref[rows, :] = (pre_act * sigmoid_value).astype(act_ref.dtype)
        out_grad = out_grad_ref[rows, :].astype(jnp.float32)
        gate = (out_grad * sigmoid_value * (1.0 + pre_act * (1.0 - sigmoid_value))).astype(jnp.bfloat16)
        aggregated_rows.append(aggregated)
        gate_rows.append(gate)

    aggregated_all = jnp.concatenate(aggregated_rows, axis=0)
    gate_all = jnp.concatenate(gate_rows, axis=0)
    wgrad_ref[...] = lax.dot_general(
        aggregated_all, gate_all, (((0,), (0,)), ((), ())), preferred_element_type=jnp.float32
    )
    if not direct_first:
        sums_ref[...] = jnp.zeros(sums_ref.shape, sums_ref.dtype)
    for g in range(panel_dev):
        back = lax.dot_general(
            gate_rows[g], weight, (((1,), (1,)), ((), ())), preferred_element_type=jnp.float32
        ).astype(jnp.bfloat16)
        for s in range(section_count):
            for k in range(slot_count):
                column, live = slot_entry(g, s, k)
                start = pl.multiple_of(column * tile_size, tile_size)
                contrib = lax.dot_general(
                    tiles_ref[g, s, k], back, (((0,), (0,)), ((), ())),
                    preferred_element_type=jnp.float32,
                )
                contrib = jnp.where(live, contrib, 0.0)
                if g == 0 and direct_first:
                    sums_ref[s, pl.ds(start, tile_size), :] = contrib
                else:
                    sums_ref[s, pl.ds(start, tile_size), :] += contrib


def layer_call(source_blocks, tiles, out_grad, weight, coords, counts):
    panel_dev, section_count, slot_count, tile_size, _ = tiles.shape
    team_rows, feature_width = source_blocks[0].shape
    kernel = functools.partial(
        layer_kernel,
        section_count=section_count,
        slot_count=slot_count,
        panel_dev=panel_dev,
        tile_size=tile_size,
    )
    smem = pl.BlockSpec(memory_space=pltpu.SMEM)
    vmem = pl.BlockSpec(memory_space=pltpu.VMEM)
    matmuls = 2 * panel_dev * section_count * slot_count + 4 * panel_dev
    return pl.pallas_call(
        kernel,
        out_shape=(
            jax.ShapeDtypeStruct(out_grad.shape, jnp.bfloat16),
            jax.ShapeDtypeStruct((feature_width, feature_width), jnp.float32),
            jax.ShapeDtypeStruct((section_count, team_rows, feature_width), jnp.float32),
        ),
        in_specs=[smem, smem] + [vmem] * (section_count + 3),
        out_specs=(vmem, vmem, vmem),
        compiler_params=pltpu.CompilerParams(vmem_limit_bytes=48 * 1024 * 1024),
        cost_estimate=pl.CostEstimate(
            flops=2 * matmuls * tile_size * tile_size * feature_width,
            transcendentals=panel_dev * tile_size * feature_width,
            bytes_accessed=tiles.size * 2 + section_count * team_rows * feature_width * 6,
        ),
    )(coords.reshape(-1), counts.reshape(-1), *source_blocks, tiles, out_grad, weight)


def swap_with(block, axis, mask):
    size = lax.axis_size(axis)
    route = [(i, i ^ mask) for i in range(size)]
    return lax.ppermute(block, axis, route)


def team_total_sum(block):
    size = lax.axis_size("team")
    rows = block.shape[0]
    if rows % size:
        return butterfly_sum(block, ("team",))
    pieces = lax.all_to_all(block.reshape(size, rows // size, -1), "team", 0, 0, tiled=True)
    own = jnp.sum(pieces, axis=0)
    copies = jnp.broadcast_to(own[None], (size,) + own.shape)
    return lax.all_to_all(copies, "team", 0, 0, tiled=True).reshape(block.shape)


def body(features, weight, out_grad, tiles, coords, counts):
    panel_dev, section_count, slot_count, tile_size, _ = tiles.shape
    team_rows, feature_width = features.shape
    reach_size = (section_count - 1) // 2
    nodes_total = team_rows * lax.axis_size("team")
    rep_size = lax.axis_size("rep")
    source_blocks = [
        features if s == reach_size else from_behind(features, "team", reach_size - s)
        for s in range(section_count)
    ]
    activated, local_weight_grad, sums = layer_call(
        source_blocks, tiles, out_grad, weight, coords, counts
    )
    if rep_size != 4:
        grad_weight = butterfly_sum(local_weight_grad, ("rep", "team"))
        share = lax.psum_scatter(sums, "rep", scatter_dimension=1, tiled=True)
        total = share[reach_size]
        for s in range(section_count):
            if s != reach_size:
                arrived = from_behind(share[s].astype(jnp.bfloat16), "team", s - reach_size)
                total = total + arrived.astype(jnp.float32)
        return (activated, grad_weight * (1.0 / math.sqrt(nodes_total)), total.astype(jnp.bfloat16))

    rep_index = lax.axis_index("rep")
    core_bit = rep_index % 2
    chip_bit = rep_index // 2
    quarter = team_rows // 4
    half_rows = 2 * quarter
    staged = sums.reshape(section_count, 2, 2, quarter, feature_width)
    kept = lax.dynamic_index_in_dim(staged, core_bit, 2, keepdims=False)
    sent = lax.dynamic_index_in_dim(staged, 1 - core_bit, 2, keepdims=False)
    packet = jnp.concatenate(
        [sent.reshape(section_count * half_rows, feature_width), local_weight_grad], axis=0
    )
    arrived = swap_with(packet, "rep", 1)
    kept = kept.reshape(section_count, half_rows, feature_width) + arrived[
        : section_count * half_rows
    ].reshape(section_count, half_rows, feature_width)
    weight_grad = team_total_sum(local_weight_grad + arrived[section_count * half_rows :])

    total = kept[reach_size]
    for s in range(section_count):
        if s != reach_size:
            moved = from_behind(kept[s].astype(jnp.bfloat16), "team", s - reach_size)
            total = total + moved.astype(jnp.float32)

    staged = total.reshape(2, quarter, feature_width)
    kept = lax.dynamic_index_in_dim(staged, chip_bit, 0, keepdims=False)
    sent = lax.dynamic_index_in_dim(staged, 1 - chip_bit, 0, keepdims=False)
    arrived = swap_with(jnp.concatenate([sent, weight_grad], axis=0), "rep", 2)
    gradient_share = (kept + arrived[:quarter]).astype(jnp.bfloat16)
    grad_weight = (weight_grad + arrived[quarter:]) * (1.0 / math.sqrt(nodes_total))
    return (activated, grad_weight, gradient_share)


def solution(mesh):
    placed = (
        P("team", None),
        P(),
        P(("team", "rep"), None),
        P(("team", "rep"), None, None, None, None),
        P(("team", "rep"), None, None),
        P(("team", "rep"), None),
    )
    return jax.shard_map(
        body,
        mesh=mesh,
        in_specs=placed,
        out_specs=(P(("team", "rep"), None), P(), P(("team", "rep"), None)),
        check_vma=False,
    )
```

```python
import functools
import math

import jax
import jax.numpy as jnp
from jax import lax
from jax.experimental import pallas as pl
from jax.experimental.pallas import tpu as pltpu
from jax.sharding import PartitionSpec as P


def from_behind(block, axis, distance):
    devices = range(lax.axis_size(axis))
    route = [((i - distance) % len(devices), i) for i in devices]
    return lax.ppermute(block, axis, route)


def butterfly_sum(block, axes):
    for axis in axes:
        size = lax.axis_size(axis)
        if size & (size - 1):
            block = lax.psum(block, axis)
            continue
        distance = 1
        while distance < size:
            route = [(i, i ^ distance) for i in range(size)]
            block = block + lax.ppermute(block, axis, route)
            distance *= 2
    return block


def neighbour_blocks(features, reach_size):
    blocks = {0: features}
    ahead_block = features
    behind_block = features
    for offset in range(1, reach_size + 1):
        ahead_block = from_behind(ahead_block, "team", -1)
        behind_block = from_behind(behind_block, "team", 1)
        blocks[offset] = ahead_block
        blocks[-offset] = behind_block
    return blocks


def layer_kernel(coords_ref, counts_ref, order_ref, *refs, section_count, slot_count, panel_dev, tile_size):
    feature_refs = refs[:section_count]
    tiles_ref, out_grad_ref, weight_ref, act_ref, wgrad_ref, sums_ref = refs[section_count:]
    weight = weight_ref[...]
    column_count = feature_refs[0].shape[0] // tile_size
    direct_first = slot_count == column_count

    def slot_entry(g, s, k):
        base = (g * section_count + s) * slot_count + k
        column = jnp.clip(coords_ref[base], 0, column_count - 1)
        live = k < counts_ref[g * section_count + s]
        return column, live

    aggregated_rows = []
    gate_rows = []
    for g in range(panel_dev):
        total = jnp.zeros((tile_size, weight.shape[1]), jnp.float32)
        for j in range(section_count):
            s = order_ref[j]
            for k in range(slot_count):
                column, live = slot_entry(g, s, k)
                start = pl.multiple_of(column * tile_size, tile_size)
                picked = feature_refs[j][pl.ds(start, tile_size), :]
                product = jnp.dot(tiles_ref[g, s, k], picked, preferred_element_type=jnp.float32)
                total = total + jnp.where(live, product, 0.0)
        aggregated = total.astype(jnp.bfloat16)
        pre_act = jnp.dot(aggregated, weight, preferred_element_type=jnp.float32)
        sigmoid_value = jax.nn.sigmoid(pre_act)
        rows = pl.ds(g * tile_size, tile_size)
        act_ref[rows, :] = (pre_act * sigmoid_value).astype(act_ref.dtype)
        out_grad = out_grad_ref[rows, :].astype(jnp.float32)
        gate = (out_grad * sigmoid_value * (1.0 + pre_act * (1.0 - sigmoid_value))).astype(jnp.bfloat16)
        aggregated_rows.append(aggregated)
        gate_rows.append(gate)

    aggregated_all = jnp.concatenate(aggregated_rows, axis=0)
    gate_all = jnp.concatenate(gate_rows, axis=0)
    wgrad_ref[...] = lax.dot_general(
        aggregated_all, gate_all, (((0,), (0,)), ((), ())), preferred_element_type=jnp.float32
    )
    if not direct_first:
        sums_ref[...] = jnp.zeros(sums_ref.shape, sums_ref.dtype)
    for g in range(panel_dev):
        back = lax.dot_general(
            gate_rows[g], weight, (((1,), (1,)), ((), ())), preferred_element_type=jnp.float32
        ).astype(jnp.bfloat16)
        for j in range(section_count):
            s = order_ref[j]
            for k in range(slot_count):
                column, live = slot_entry(g, s, k)
                start = pl.multiple_of(column * tile_size, tile_size)
                contrib = lax.dot_general(
                    tiles_ref[g, s, k], back, (((0,), (0,)), ((), ())),
                    preferred_element_type=jnp.float32,
                )
                contrib = jnp.where(live, contrib, 0.0)
                if g == 0 and direct_first:
                    sums_ref[s, pl.ds(start, tile_size), :] = contrib
                else:
                    sums_ref[s, pl.ds(start, tile_size), :] += contrib


def layer_call(source_blocks, order, tiles, out_grad, weight, coords, counts):
    panel_dev, section_count, slot_count, tile_size, _ = tiles.shape
    team_rows, feature_width = source_blocks[0].shape
    kernel = functools.partial(
        layer_kernel,
        section_count=section_count,
        slot_count=slot_count,
        panel_dev=panel_dev,
        tile_size=tile_size,
    )
    smem = pl.BlockSpec(memory_space=pltpu.SMEM)
    vmem = pl.BlockSpec(memory_space=pltpu.VMEM)
    matmuls = 2 * panel_dev * section_count * slot_count + 4 * panel_dev
    return pl.pallas_call(
        kernel,
        out_shape=(
            jax.ShapeDtypeStruct(out_grad.shape, jnp.bfloat16),
            jax.ShapeDtypeStruct((feature_width, feature_width), jnp.float32),
            jax.ShapeDtypeStruct((section_count, team_rows, feature_width), jnp.float32),
        ),
        in_specs=[smem, smem, smem] + [vmem] * (section_count + 3),
        out_specs=(vmem, vmem, vmem),
        compiler_params=pltpu.CompilerParams(vmem_limit_bytes=48 * 1024 * 1024),
        cost_estimate=pl.CostEstimate(
            flops=2 * matmuls * tile_size * tile_size * feature_width,
            transcendentals=panel_dev * tile_size * feature_width,
            bytes_accessed=tiles.size * 2 + section_count * team_rows * feature_width * 6,
        ),
    )(coords.reshape(-1), counts.reshape(-1), order, *source_blocks, tiles, out_grad, weight)


def swap_with(block, axis, mask):
    size = lax.axis_size(axis)
    route = [(i, i ^ mask) for i in range(size)]
    return lax.ppermute(block, axis, route)


def team_total_sum(block):
    size = lax.axis_size("team")
    rows = block.shape[0]
    if rows % size:
        return butterfly_sum(block, ("team",))
    pieces = lax.all_to_all(block.reshape(size, rows // size, -1), "team", 0, 0, tiled=True)
    own = jnp.sum(pieces, axis=0)
    copies = jnp.broadcast_to(own[None], (size,) + own.shape)
    return lax.all_to_all(copies, "team", 0, 0, tiled=True).reshape(block.shape)


def gather_sources(features, reach_size, rep_size):
    team_size = lax.axis_size("team")
    if rep_size % 2:
        blocks = [features] + [
            from_behind(features, "team", -shift)
            for shift in range(-reach_size, reach_size + 1)
            if shift
        ]
        shifts = [0] + [shift for shift in range(-reach_size, reach_size + 1) if shift]
        order = jnp.array([reach_size + shift for shift in shifts], jnp.int32)
        return blocks, order
    sign = 1 - 2 * (lax.axis_index("rep") % 2)
    fetched = []
    for distance in range(1, reach_size + 1):
        route = []
        for team in range(team_size):
            for rep in range(rep_size):
                step = distance if rep % 2 == 0 else -distance
                source = ((team + step) % team_size) * rep_size + rep
                route.append((source, team * rep_size + rep))
        fetched.append(lax.ppermute(features, ("team", "rep"), route))
    swapped = swap_with(jnp.stack(fetched), "rep", 1)
    blocks = [features] + fetched + [swapped[i] for i in range(reach_size)]
    distances = jnp.arange(1, reach_size + 1, dtype=jnp.int32)
    order = jnp.concatenate(
        [jnp.array([reach_size], jnp.int32), reach_size + sign * distances, reach_size - sign * distances]
    ).astype(jnp.int32)
    return blocks, order


def body(features, weight, out_grad, tiles, coords, counts):
    panel_dev, section_count, slot_count, tile_size, _ = tiles.shape
    team_rows, feature_width = features.shape
    reach_size = (section_count - 1) // 2
    nodes_total = team_rows * lax.axis_size("team")
    rep_size = lax.axis_size("rep")
    source_blocks, order = gather_sources(features, reach_size, rep_size)
    activated, local_weight_grad, sums = layer_call(
        source_blocks, order, tiles, out_grad, weight, coords, counts
    )
    if rep_size != 4:
        grad_weight = butterfly_sum(local_weight_grad, ("rep", "team"))
        share = lax.psum_scatter(sums, "rep", scatter_dimension=1, tiled=True)
        total = share[reach_size]
        for s in range(section_count):
            if s != reach_size:
                arrived = from_behind(share[s].astype(jnp.bfloat16), "team", s - reach_size)
                total = total + arrived.astype(jnp.float32)
        return (activated, grad_weight * (1.0 / math.sqrt(nodes_total)), total.astype(jnp.bfloat16))

    rep_index = lax.axis_index("rep")
    core_bit = rep_index % 2
    chip_bit = rep_index // 2
    quarter = team_rows // 4
    half_rows = 2 * quarter
    staged = sums.reshape(section_count, 2, 2, quarter, feature_width)
    kept = lax.dynamic_index_in_dim(staged, core_bit, 2, keepdims=False)
    sent = lax.dynamic_index_in_dim(staged, 1 - core_bit, 2, keepdims=False)
    packet = jnp.concatenate(
        [sent.reshape(section_count * half_rows, feature_width), local_weight_grad], axis=0
    )
    arrived = swap_with(packet, "rep", 1)
    kept = kept.reshape(section_count, half_rows, feature_width) + arrived[
        : section_count * half_rows
    ].reshape(section_count, half_rows, feature_width)
    weight_grad = team_total_sum(local_weight_grad + arrived[section_count * half_rows :])

    total = kept[reach_size]
    for s in range(section_count):
        if s != reach_size:
            moved = from_behind(kept[s].astype(jnp.bfloat16), "team", s - reach_size)
            total = total + moved.astype(jnp.float32)

    staged = total.reshape(2, quarter, feature_width)
    kept = lax.dynamic_index_in_dim(staged, chip_bit, 0, keepdims=False)
    sent = lax.dynamic_index_in_dim(staged, 1 - chip_bit, 0, keepdims=False)
    arrived = swap_with(jnp.concatenate([sent, weight_grad], axis=0), "rep", 2)
    gradient_share = (kept + arrived[:quarter]).astype(jnp.bfloat16)
    grad_weight = (weight_grad + arrived[quarter:]) * (1.0 / math.sqrt(nodes_total))
    return (activated, grad_weight, gradient_share)


def solution(mesh):
    placed = (
        P("team", None),
        P(),
        P(("team", "rep"), None),
        P(("team", "rep"), None, None, None, None),
        P(("team", "rep"), None, None),
        P(("team", "rep"), None),
    )
    return jax.shard_map(
        body,
        mesh=mesh,
        in_specs=placed,
        out_specs=(P(("team", "rep"), None), P(), P(("team", "rep"), None)),
        check_vma=False,
    )
```

```python
import functools
import math

import jax
import jax.numpy as jnp
from jax import lax
from jax.experimental import pallas as pl
from jax.experimental.pallas import tpu as pltpu
from jax.sharding import PartitionSpec as P


def from_behind(block, axis, distance):
    devices = range(lax.axis_size(axis))
    route = [((i - distance) % len(devices), i) for i in devices]
    return lax.ppermute(block, axis, route)


def butterfly_sum(block, axes):
    for axis in axes:
        size = lax.axis_size(axis)
        if size & (size - 1):
            block = lax.psum(block, axis)
            continue
        distance = 1
        while distance < size:
            route = [(i, i ^ distance) for i in range(size)]
            block = block + lax.ppermute(block, axis, route)
            distance *= 2
    return block


def neighbour_blocks(features, reach_size):
    blocks = {0: features}
    ahead_block = features
    behind_block = features
    for offset in range(1, reach_size + 1):
        ahead_block = from_behind(ahead_block, "team", -1)
        behind_block = from_behind(behind_block, "team", 1)
        blocks[offset] = ahead_block
        blocks[-offset] = behind_block
    return blocks


def layer_kernel(coords_ref, counts_ref, order_ref, *refs, section_count, slot_count, panel_dev, tile_size):
    feature_refs = refs[:section_count]
    tiles_ref, out_grad_ref, weight_ref, act_ref, wgrad_ref, sums_ref = refs[section_count:]
    weight = weight_ref[...]
    column_count = feature_refs[0].shape[0] // tile_size
    direct_first = slot_count == column_count

    def slot_entry(g, s, k):
        base = (g * section_count + s) * slot_count + k
        column = jnp.clip(coords_ref[base], 0, column_count - 1)
        live = k < counts_ref[g * section_count + s]
        return column, live

    aggregated_rows = []
    gate_rows = []
    for g in range(panel_dev):
        total = jnp.zeros((tile_size, weight.shape[1]), jnp.float32)
        for j in range(section_count):
            s = order_ref[j]
            for k in range(slot_count):
                column, live = slot_entry(g, s, k)
                start = pl.multiple_of(column * tile_size, tile_size)
                picked = feature_refs[j][pl.ds(start, tile_size), :]
                product = jnp.dot(tiles_ref[g, s, k], picked, preferred_element_type=jnp.float32)
                total = total + jnp.where(live, product, 0.0)
        aggregated = total.astype(jnp.bfloat16)
        pre_act = jnp.dot(aggregated, weight, preferred_element_type=jnp.float32)
        sigmoid_value = jax.nn.sigmoid(pre_act)
        rows = pl.ds(g * tile_size, tile_size)
        act_ref[rows, :] = (pre_act * sigmoid_value).astype(act_ref.dtype)
        out_grad = out_grad_ref[rows, :].astype(jnp.float32)
        gate = (out_grad * sigmoid_value * (1.0 + pre_act * (1.0 - sigmoid_value))).astype(jnp.bfloat16)
        aggregated_rows.append(aggregated)
        gate_rows.append(gate)

    aggregated_all = jnp.concatenate(aggregated_rows, axis=0)
    gate_all = jnp.concatenate(gate_rows, axis=0)
    wgrad_ref[...] = lax.dot_general(
        aggregated_all, gate_all, (((0,), (0,)), ((), ())), preferred_element_type=jnp.float32
    )
    if not direct_first:
        sums_ref[...] = jnp.zeros(sums_ref.shape, sums_ref.dtype)
    for g in range(panel_dev):
        back = lax.dot_general(
            gate_rows[g], weight, (((1,), (1,)), ((), ())), preferred_element_type=jnp.float32
        ).astype(jnp.bfloat16)
        for j in range(section_count):
            s = order_ref[j]
            for k in range(slot_count):
                column, live = slot_entry(g, s, k)
                start = pl.multiple_of(column * tile_size, tile_size)
                contrib = lax.dot_general(
                    tiles_ref[g, s, k], back, (((0,), (0,)), ((), ())),
                    preferred_element_type=jnp.float32,
                )
                contrib = jnp.where(live, contrib, 0.0)
                if g == 0 and direct_first:
                    sums_ref[s, pl.ds(start, tile_size), :] = contrib
                else:
                    sums_ref[s, pl.ds(start, tile_size), :] += contrib


def layer_call(source_blocks, order, tiles, out_grad, weight, coords, counts):
    panel_dev, section_count, slot_count, tile_size, _ = tiles.shape
    team_rows, feature_width = source_blocks[0].shape
    kernel = functools.partial(
        layer_kernel,
        section_count=section_count,
        slot_count=slot_count,
        panel_dev=panel_dev,
        tile_size=tile_size,
    )
    smem = pl.BlockSpec(memory_space=pltpu.SMEM)
    vmem = pl.BlockSpec(memory_space=pltpu.VMEM)
    matmuls = 2 * panel_dev * section_count * slot_count + 4 * panel_dev
    return pl.pallas_call(
        kernel,
        out_shape=(
            jax.ShapeDtypeStruct(out_grad.shape, jnp.bfloat16),
            jax.ShapeDtypeStruct((feature_width, feature_width), jnp.float32),
            jax.ShapeDtypeStruct((section_count, team_rows, feature_width), jnp.float32),
        ),
        in_specs=[smem, smem, smem] + [vmem] * (section_count + 3),
        out_specs=(vmem, vmem, vmem),
        compiler_params=pltpu.CompilerParams(vmem_limit_bytes=48 * 1024 * 1024),
        cost_estimate=pl.CostEstimate(
            flops=2 * matmuls * tile_size * tile_size * feature_width,
            transcendentals=panel_dev * tile_size * feature_width,
            bytes_accessed=tiles.size * 2 + section_count * team_rows * feature_width * 6,
        ),
    )(coords.reshape(-1), counts.reshape(-1), order, *source_blocks, tiles, out_grad, weight)


def swap_with(block, axis, mask):
    size = lax.axis_size(axis)
    route = [(i, i ^ mask) for i in range(size)]
    return lax.ppermute(block, axis, route)


def team_total_sum(block):
    size = lax.axis_size("team")
    rows = block.shape[0]
    if rows % size:
        return butterfly_sum(block, ("team",))
    pieces = lax.all_to_all(block.reshape(size, rows // size, -1), "team", 0, 0, tiled=True)
    own = jnp.sum(pieces, axis=0)
    copies = jnp.broadcast_to(own[None], (size,) + own.shape)
    return lax.all_to_all(copies, "team", 0, 0, tiled=True).reshape(block.shape)


def gather_sources(features, reach_size, rep_size):
    team_size = lax.axis_size("team")
    if rep_size % 2:
        blocks = [features] + [
            from_behind(features, "team", -shift)
            for shift in range(-reach_size, reach_size + 1)
            if shift
        ]
        shifts = [0] + [shift for shift in range(-reach_size, reach_size + 1) if shift]
        order = jnp.array([reach_size + shift for shift in shifts], jnp.int32)
        return blocks, order
    sign = 1 - 2 * (lax.axis_index("rep") % 2)
    fetched = []
    for distance in range(1, reach_size + 1):
        route = []
        for team in range(team_size):
            for rep in range(rep_size):
                step = distance if rep % 2 == 0 else -distance
                source = ((team + step) % team_size) * rep_size + rep
                route.append((source, team * rep_size + rep))
        fetched.append(lax.ppermute(features, ("team", "rep"), route))
    swapped = swap_with(jnp.stack(fetched), "rep", 1)
    blocks = [features] + fetched + [swapped[i] for i in range(reach_size)]
    distances = jnp.arange(1, reach_size + 1, dtype=jnp.int32)
    order = jnp.concatenate(
        [jnp.array([reach_size], jnp.int32), reach_size + sign * distances, reach_size - sign * distances]
    ).astype(jnp.int32)
    return blocks, order


def body(features, weight, out_grad, tiles, coords, counts):
    panel_dev, section_count, slot_count, tile_size, _ = tiles.shape
    team_rows, feature_width = features.shape
    reach_size = (section_count - 1) // 2
    nodes_total = team_rows * lax.axis_size("team")
    rep_size = lax.axis_size("rep")
    source_blocks, order = gather_sources(features, reach_size, rep_size)
    activated, local_weight_grad, sums = layer_call(
        source_blocks, order, tiles, out_grad, weight, coords, counts
    )
    if rep_size != 4:
        grad_weight = butterfly_sum(local_weight_grad, ("rep", "team"))
        share = lax.psum_scatter(sums, "rep", scatter_dimension=1, tiled=True)
        total = share[reach_size]
        for s in range(section_count):
            if s != reach_size:
                arrived = from_behind(share[s].astype(jnp.bfloat16), "team", s - reach_size)
                total = total + arrived.astype(jnp.float32)
        return (activated, grad_weight * (1.0 / math.sqrt(nodes_total)), total.astype(jnp.bfloat16))

    rep_index = lax.axis_index("rep")
    core_bit = rep_index % 2
    chip_bit = rep_index // 2
    team_size = lax.axis_size("team")
    quarter = team_rows // 4
    half_rows = 2 * quarter

    given = lax.dynamic_slice_in_dim(sums, core_bit * (reach_size + 1), reach_size, 0)
    mine = lax.dynamic_slice_in_dim(sums, (1 - core_bit) * (reach_size + 1), reach_size, 0)
    local = sums[reach_size].reshape(2, 2, quarter, feature_width)
    local_kept = lax.dynamic_index_in_dim(local, core_bit, 1, keepdims=False)
    local_given = lax.dynamic_index_in_dim(local, 1 - core_bit, 1, keepdims=False)
    packet = jnp.concatenate(
        [
            given.reshape(reach_size * team_rows, feature_width),
            local_given.reshape(half_rows, feature_width),
            local_weight_grad,
        ],
        axis=0,
    )
    arrived = swap_with(packet, "rep", 1)
    cut = reach_size * team_rows
    mine = mine + arrived[:cut].reshape(reach_size, team_rows, feature_width)
    local_kept = local_kept + arrived[cut : cut + half_rows].reshape(2, quarter, feature_width)
    weight_grad = team_total_sum(local_weight_grad + arrived[cut + half_rows :])

    incoming = None
    for index in range(reach_size):
        distance = index + 1
        pick = index + core_bit * (reach_size - 1 - 2 * index)
        block = lax.dynamic_index_in_dim(mine, pick, 0, keepdims=False).astype(jnp.bfloat16)
        route = []
        for team in range(team_size):
            for rep in range(rep_size):
                step = distance if rep % 2 == 0 else -distance
                route.append((team * rep_size + rep, ((team + step) % team_size) * rep_size + rep))
        moved = lax.ppermute(block, ("team", "rep"), route).astype(jnp.float32)
        incoming = moved if incoming is None else incoming + moved

    staged = incoming.reshape(2, 2, quarter, feature_width)
    kept = lax.dynamic_index_in_dim(staged, core_bit, 1, keepdims=False)
    sent = lax.dynamic_index_in_dim(staged, 1 - core_bit, 1, keepdims=False)
    total = kept + local_kept + swap_with(sent, "rep", 1)

    kept = lax.dynamic_index_in_dim(total, chip_bit, 0, keepdims=False)
    sent = lax.dynamic_index_in_dim(total, 1 - chip_bit, 0, keepdims=False)
    arrived = swap_with(jnp.concatenate([sent, weight_grad], axis=0), "rep", 2)
    gradient_share = (kept + arrived[:quarter]).astype(jnp.bfloat16)
    grad_weight = (weight_grad + arrived[quarter:]) * (1.0 / math.sqrt(nodes_total))
    return (activated, grad_weight, gradient_share)


def solution(mesh):
    placed = (
        P("team", None),
        P(),
        P(("team", "rep"), None),
        P(("team", "rep"), None, None, None, None),
        P(("team", "rep"), None, None),
        P(("team", "rep"), None),
    )
    return jax.shard_map(
        body,
        mesh=mesh,
        in_specs=placed,
        out_specs=(P(("team", "rep"), None), P(), P(("team", "rep"), None)),
        check_vma=False,
    )
```

```python
import functools
import math

import jax
import jax.numpy as jnp
from jax import lax
from jax.experimental import pallas as pl
from jax.experimental.pallas import tpu as pltpu
from jax.sharding import PartitionSpec as P


def from_behind(block, axis, distance):
    devices = range(lax.axis_size(axis))
    route = [((i - distance) % len(devices), i) for i in devices]
    return lax.ppermute(block, axis, route)


def butterfly_sum(block, axes):
    for axis in axes:
        size = lax.axis_size(axis)
        if size & (size - 1):
            block = lax.psum(block, axis)
            continue
        distance = 1
        while distance < size:
            route = [(i, i ^ distance) for i in range(size)]
            block = block + lax.ppermute(block, axis, route)
            distance *= 2
    return block


def neighbour_blocks(features, reach_size):
    blocks = {0: features}
    ahead_block = features
    behind_block = features
    for offset in range(1, reach_size + 1):
        ahead_block = from_behind(ahead_block, "team", -1)
        behind_block = from_behind(behind_block, "team", 1)
        blocks[offset] = ahead_block
        blocks[-offset] = behind_block
    return blocks


def layer_kernel(coords_ref, counts_ref, order_ref, *refs, section_count, slot_count, panel_dev, tile_size):
    feature_refs = refs[:section_count]
    tiles_ref, out_grad_ref, weight_ref, act_ref, wgrad_ref, sums_ref = refs[section_count:]
    weight = weight_ref[...]
    column_count = feature_refs[0].shape[0] // tile_size
    direct_first = slot_count == column_count

    def slot_entry(g, s, k):
        base = (g * section_count + s) * slot_count + k
        column = jnp.clip(coords_ref[base], 0, column_count - 1)
        live = k < counts_ref[g * section_count + s]
        return column, live

    aggregated_rows = []
    gate_rows = []
    for g in range(panel_dev):
        total = jnp.zeros((tile_size, weight.shape[1]), jnp.float32)
        for j in range(section_count):
            s = order_ref[j]
            for k in range(slot_count):
                column, live = slot_entry(g, s, k)
                start = pl.multiple_of(column * tile_size, tile_size)
                picked = feature_refs[j][pl.ds(start, tile_size), :]
                product = jnp.dot(tiles_ref[g, s, k], picked, preferred_element_type=jnp.float32)
                total = total + jnp.where(live, product, 0.0)
        aggregated = total.astype(jnp.bfloat16)
        pre_act = jnp.dot(aggregated, weight, preferred_element_type=jnp.float32)
        sigmoid_value = jax.nn.sigmoid(pre_act)
        rows = pl.ds(g * tile_size, tile_size)
        act_ref[rows, :] = (pre_act * sigmoid_value).astype(act_ref.dtype)
        out_grad = out_grad_ref[rows, :].astype(jnp.float32)
        gate = (out_grad * sigmoid_value * (1.0 + pre_act * (1.0 - sigmoid_value))).astype(jnp.bfloat16)
        aggregated_rows.append(aggregated)
        gate_rows.append(gate)

    aggregated_all = jnp.concatenate(aggregated_rows, axis=0)
    gate_all = jnp.concatenate(gate_rows, axis=0)
    wgrad_ref[...] = lax.dot_general(
        aggregated_all, gate_all, (((0,), (0,)), ((), ())), preferred_element_type=jnp.float32
    )
    if not direct_first:
        sums_ref[...] = jnp.zeros(sums_ref.shape, sums_ref.dtype)
    for g in range(panel_dev):
        back = lax.dot_general(
            gate_rows[g], weight, (((1,), (1,)), ((), ())), preferred_element_type=jnp.float32
        ).astype(jnp.bfloat16)
        for j in range(section_count):
            s = order_ref[j]
            for k in range(slot_count):
                column, live = slot_entry(g, s, k)
                start = pl.multiple_of(column * tile_size, tile_size)
                contrib = lax.dot_general(
                    tiles_ref[g, s, k], back, (((0,), (0,)), ((), ())),
                    preferred_element_type=jnp.float32,
                )
                contrib = jnp.where(live, contrib, 0.0)
                if g == 0 and direct_first:
                    sums_ref[s, pl.ds(start, tile_size), :] = contrib
                else:
                    sums_ref[s, pl.ds(start, tile_size), :] += contrib


def layer_call(source_blocks, order, tiles, out_grad, weight, coords, counts):
    panel_dev, section_count, slot_count, tile_size, _ = tiles.shape
    team_rows, feature_width = source_blocks[0].shape
    kernel = functools.partial(
        layer_kernel,
        section_count=section_count,
        slot_count=slot_count,
        panel_dev=panel_dev,
        tile_size=tile_size,
    )
    smem = pl.BlockSpec(memory_space=pltpu.SMEM)
    vmem = pl.BlockSpec(memory_space=pltpu.VMEM)
    matmuls = 2 * panel_dev * section_count * slot_count + 4 * panel_dev
    return pl.pallas_call(
        kernel,
        out_shape=(
            jax.ShapeDtypeStruct(out_grad.shape, jnp.bfloat16),
            jax.ShapeDtypeStruct((feature_width, feature_width), jnp.float32),
            jax.ShapeDtypeStruct((section_count, team_rows, feature_width), jnp.float32),
        ),
        in_specs=[smem, smem, smem] + [vmem] * (section_count + 3),
        out_specs=(vmem, vmem, vmem),
        compiler_params=pltpu.CompilerParams(vmem_limit_bytes=48 * 1024 * 1024),
        cost_estimate=pl.CostEstimate(
            flops=2 * matmuls * tile_size * tile_size * feature_width,
            transcendentals=panel_dev * tile_size * feature_width,
            bytes_accessed=tiles.size * 2 + section_count * team_rows * feature_width * 6,
        ),
    )(coords.reshape(-1), counts.reshape(-1), order, *source_blocks, tiles, out_grad, weight)


def swap_with(block, axis, mask):
    size = lax.axis_size(axis)
    route = [(i, i ^ mask) for i in range(size)]
    return lax.ppermute(block, axis, route)


def team_scatter_sum(block):
    size = lax.axis_size("team")
    rows = block.shape[0]
    pieces = lax.all_to_all(block.reshape(size, rows // size, -1), "team", 0, 0, tiled=True)
    return jnp.sum(pieces, axis=0)


def team_gather(piece):
    size = lax.axis_size("team")
    copies = jnp.broadcast_to(piece[None], (size,) + piece.shape)
    gathered = lax.all_to_all(copies, "team", 0, 0, tiled=True)
    return gathered.reshape(size * piece.shape[0], -1)


def gather_sources(features, reach_size, rep_size):
    team_size = lax.axis_size("team")
    if rep_size % 2:
        blocks = [features] + [
            from_behind(features, "team", -shift)
            for shift in range(-reach_size, reach_size + 1)
            if shift
        ]
        shifts = [0] + [shift for shift in range(-reach_size, reach_size + 1) if shift]
        order = jnp.array([reach_size + shift for shift in shifts], jnp.int32)
        return blocks, order
    sign = 1 - 2 * (lax.axis_index("rep") % 2)
    fetched = []
    for distance in range(1, reach_size + 1):
        route = []
        for team in range(team_size):
            for rep in range(rep_size):
                step = distance if rep % 2 == 0 else -distance
                source = ((team + step) % team_size) * rep_size + rep
                route.append((source, team * rep_size + rep))
        fetched.append(lax.ppermute(features, ("team", "rep"), route))
    swapped = swap_with(jnp.stack(fetched), "rep", 1)
    blocks = [features] + fetched + [swapped[i] for i in range(reach_size)]
    distances = jnp.arange(1, reach_size + 1, dtype=jnp.int32)
    order = jnp.concatenate(
        [jnp.array([reach_size], jnp.int32), reach_size + sign * distances, reach_size - sign * distances]
    ).astype(jnp.int32)
    return blocks, order


def body(features, weight, out_grad, tiles, coords, counts):
    panel_dev, section_count, slot_count, tile_size, _ = tiles.shape
    team_rows, feature_width = features.shape
    reach_size = (section_count - 1) // 2
    nodes_total = team_rows * lax.axis_size("team")
    rep_size = lax.axis_size("rep")
    source_blocks, order = gather_sources(features, reach_size, rep_size)
    activated, local_weight_grad, sums = layer_call(
        source_blocks, order, tiles, out_grad, weight, coords, counts
    )
    if rep_size != 4:
        grad_weight = butterfly_sum(local_weight_grad, ("rep", "team"))
        share = lax.psum_scatter(sums, "rep", scatter_dimension=1, tiled=True)
        total = share[reach_size]
        for s in range(section_count):
            if s != reach_size:
                arrived = from_behind(share[s].astype(jnp.bfloat16), "team", s - reach_size)
                total = total + arrived.astype(jnp.float32)
        return (activated, grad_weight * (1.0 / math.sqrt(nodes_total)), total.astype(jnp.bfloat16))

    rep_index = lax.axis_index("rep")
    core_bit = rep_index % 2
    chip_bit = rep_index // 2
    quarter = team_rows // 4
    half_rows = 2 * quarter
    staged = sums.reshape(section_count, 2, 2, quarter, feature_width)
    kept = lax.dynamic_index_in_dim(staged, core_bit, 2, keepdims=False)
    sent = lax.dynamic_index_in_dim(staged, 1 - core_bit, 2, keepdims=False)
    packet = jnp.concatenate(
        [sent.reshape(section_count * half_rows, feature_width), local_weight_grad], axis=0
    )
    arrived = swap_with(packet, "rep", 1)
    kept = kept.reshape(section_count, half_rows, feature_width) + arrived[
        : section_count * half_rows
    ].reshape(section_count, half_rows, feature_width)
    weight_grad = team_scatter_sum(local_weight_grad + arrived[section_count * half_rows :])

    total = kept[reach_size]
    for s in range(section_count):
        if s != reach_size:
            moved = from_behind(kept[s].astype(jnp.bfloat16), "team", s - reach_size)
            total = total + moved.astype(jnp.float32)

    staged = total.reshape(2, quarter, feature_width)
    kept = lax.dynamic_index_in_dim(staged, chip_bit, 0, keepdims=False)
    sent = lax.dynamic_index_in_dim(staged, 1 - chip_bit, 0, keepdims=False)
    arrived = swap_with(jnp.concatenate([sent, weight_grad], axis=0), "rep", 2)
    gradient_share = (kept + arrived[:quarter]).astype(jnp.bfloat16)
    grad_weight = team_gather(weight_grad + arrived[quarter:]) * (1.0 / math.sqrt(nodes_total))
    return (activated, grad_weight, gradient_share)


def solution(mesh):
    placed = (
        P("team", None),
        P(),
        P(("team", "rep"), None),
        P(("team", "rep"), None, None, None, None),
        P(("team", "rep"), None, None),
        P(("team", "rep"), None),
    )
    return jax.shard_map(
        body,
        mesh=mesh,
        in_specs=placed,
        out_specs=(P(("team", "rep"), None), P(), P(("team", "rep"), None)),
        check_vma=False,
    )
```

```python
import functools
import math

import jax
import jax.numpy as jnp
from jax import lax
from jax.experimental import pallas as pl
from jax.experimental.pallas import tpu as pltpu
from jax.sharding import PartitionSpec as P


def from_behind(block, axis, distance):
    devices = range(lax.axis_size(axis))
    route = [((i - distance) % len(devices), i) for i in devices]
    return lax.ppermute(block, axis, route)


def butterfly_sum(block, axes):
    for axis in axes:
        size = lax.axis_size(axis)
        if size & (size - 1):
            block = lax.psum(block, axis)
            continue
        distance = 1
        while distance < size:
            route = [(i, i ^ distance) for i in range(size)]
            block = block + lax.ppermute(block, axis, route)
            distance *= 2
    return block


def layer_kernel(coords_ref, counts_ref, order_ref, *refs, section_count, slot_count, panel_dev, tile_size):
    feature_refs = refs[:section_count]
    tiles_ref, out_grad_ref, weight_ref, act_ref, wgrad_ref, sums_ref = refs[section_count:]
    weight = weight_ref[...]
    column_count = feature_refs[0].shape[0] // tile_size
    direct_first = slot_count == column_count

    def slot_entry(g, s, k):
        base = (g * section_count + s) * slot_count + k
        column = jnp.clip(coords_ref[base], 0, column_count - 1)
        live = k < counts_ref[g * section_count + s]
        return column, live

    aggregated_rows = []
    gate_rows = []
    for g in range(panel_dev):
        total = jnp.zeros((tile_size, weight.shape[1]), jnp.float32)
        for j in range(section_count):
            s = order_ref[j]
            for k in range(slot_count):
                column, live = slot_entry(g, s, k)
                start = pl.multiple_of(column * tile_size, tile_size)
                picked = feature_refs[j][pl.ds(start, tile_size), :]
                product = jnp.dot(tiles_ref[g, s, k], picked, preferred_element_type=jnp.float32)
                total = total + jnp.where(live, product, 0.0)
        aggregated = total.astype(jnp.bfloat16)
        pre_act = jnp.dot(aggregated, weight, preferred_element_type=jnp.float32)
        sigmoid_value = jax.nn.sigmoid(pre_act)
        rows = pl.ds(g * tile_size, tile_size)
        act_ref[rows, :] = (pre_act * sigmoid_value).astype(act_ref.dtype)
        out_grad = out_grad_ref[rows, :].astype(jnp.float32)
        gate = (out_grad * sigmoid_value * (1.0 + pre_act * (1.0 - sigmoid_value))).astype(jnp.bfloat16)
        aggregated_rows.append(aggregated)
        gate_rows.append(gate)

    aggregated_all = jnp.concatenate(aggregated_rows, axis=0)
    gate_all = jnp.concatenate(gate_rows, axis=0)
    wgrad_ref[...] = lax.dot_general(
        aggregated_all, gate_all, (((0,), (0,)), ((), ())), preferred_element_type=jnp.float32
    )
    if not direct_first:
        sums_ref[...] = jnp.zeros(sums_ref.shape, sums_ref.dtype)
    for g in range(panel_dev):
        back = lax.dot_general(
            gate_rows[g], weight, (((1,), (1,)), ((), ())), preferred_element_type=jnp.float32
        ).astype(jnp.bfloat16)
        for j in range(section_count):
            s = order_ref[j]
            for k in range(slot_count):
                column, live = slot_entry(g, s, k)
                start = pl.multiple_of(column * tile_size, tile_size)
                contrib = lax.dot_general(
                    tiles_ref[g, s, k], back, (((0,), (0,)), ((), ())),
                    preferred_element_type=jnp.float32,
                )
                contrib = jnp.where(live, contrib, 0.0)
                if g == 0 and direct_first:
                    sums_ref[s, pl.ds(start, tile_size), :] = contrib
                else:
                    sums_ref[s, pl.ds(start, tile_size), :] += contrib


def layer_call(source_blocks, order, tiles, out_grad, weight, coords, counts):
    panel_dev, section_count, slot_count, tile_size, _ = tiles.shape
    team_rows, feature_width = source_blocks[0].shape
    kernel = functools.partial(
        layer_kernel,
        section_count=section_count,
        slot_count=slot_count,
        panel_dev=panel_dev,
        tile_size=tile_size,
    )
    smem = pl.BlockSpec(memory_space=pltpu.SMEM)
    vmem = pl.BlockSpec(memory_space=pltpu.VMEM)
    matmuls = 2 * panel_dev * section_count * slot_count + 4 * panel_dev
    return pl.pallas_call(
        kernel,
        out_shape=(
            jax.ShapeDtypeStruct(out_grad.shape, jnp.bfloat16),
            jax.ShapeDtypeStruct((feature_width, feature_width), jnp.float32),
            jax.ShapeDtypeStruct((section_count, team_rows, feature_width), jnp.float32),
        ),
        in_specs=[smem, smem, smem] + [vmem] * (section_count + 3),
        out_specs=(vmem, vmem, vmem),
        compiler_params=pltpu.CompilerParams(vmem_limit_bytes=48 * 1024 * 1024),
        cost_estimate=pl.CostEstimate(
            flops=2 * matmuls * tile_size * tile_size * feature_width,
            transcendentals=panel_dev * tile_size * feature_width,
            bytes_accessed=tiles.size * 2 + section_count * team_rows * feature_width * 6,
        ),
    )(coords.reshape(-1), counts.reshape(-1), order, *source_blocks, tiles, out_grad, weight)


def swap_with(block, axis, mask):
    size = lax.axis_size(axis)
    route = [(i, i ^ mask) for i in range(size)]
    return lax.ppermute(block, axis, route)


def team_scatter_sum(block):
    size = lax.axis_size("team")
    rows = block.shape[0]
    pieces = lax.all_to_all(block.reshape(size, rows // size, -1), "team", 0, 0, tiled=True)
    return jnp.sum(pieces, axis=0)


def team_gather(piece):
    size = lax.axis_size("team")
    copies = jnp.broadcast_to(piece[None], (size,) + piece.shape)
    gathered = lax.all_to_all(copies, "team", 0, 0, tiled=True)
    return gathered.reshape(size * piece.shape[0], -1)


def gather_sources(features, reach_size, rep_size):
    team_size = lax.axis_size("team")
    if rep_size % 2:
        blocks = [features] + [
            from_behind(features, "team", -shift)
            for shift in range(-reach_size, reach_size + 1)
            if shift
        ]
        shifts = [0] + [shift for shift in range(-reach_size, reach_size + 1) if shift]
        order = jnp.array([reach_size + shift for shift in shifts], jnp.int32)
        return blocks, order
    sign = 1 - 2 * (lax.axis_index("rep") % 2)
    fetched = []
    for distance in range(1, reach_size + 1):
        route = []
        for team in range(team_size):
            for rep in range(rep_size):
                step = distance if rep % 2 == 0 else -distance
                source = ((team + step) % team_size) * rep_size + rep
                route.append((source, team * rep_size + rep))
        fetched.append(lax.ppermute(features, ("team", "rep"), route))
    swapped = swap_with(jnp.stack(fetched), "rep", 1)
    blocks = [features] + fetched + [swapped[i] for i in range(reach_size)]
    distances = jnp.arange(1, reach_size + 1, dtype=jnp.int32)
    order = jnp.concatenate(
        [jnp.array([reach_size], jnp.int32), reach_size + sign * distances, reach_size - sign * distances]
    ).astype(jnp.int32)
    return blocks, order


def body(features, weight, out_grad, tiles, coords, counts):
    _, section_count, _, _, _ = tiles.shape
    team_rows, feature_width = features.shape
    reach_size = (section_count - 1) // 2
    nodes_total = team_rows * lax.axis_size("team")
    rep_size = lax.axis_size("rep")
    source_blocks, order = gather_sources(features, reach_size, rep_size)
    activated, local_weight_grad, sums = layer_call(
        source_blocks, order, tiles, out_grad, weight, coords, counts
    )
    if rep_size != 4:
        grad_weight = butterfly_sum(local_weight_grad, ("rep", "team"))
        share = lax.psum_scatter(sums, "rep", scatter_dimension=1, tiled=True)
        total = share[reach_size]
        for s in range(section_count):
            if s != reach_size:
                arrived = from_behind(share[s].astype(jnp.bfloat16), "team", s - reach_size)
                total = total + arrived.astype(jnp.float32)
        return (activated, grad_weight * (1.0 / math.sqrt(nodes_total)), total.astype(jnp.bfloat16))

    rep_index = lax.axis_index("rep")
    core_bit = rep_index % 2
    chip_bit = rep_index // 2
    quarter = team_rows // 4
    half_rows = 2 * quarter
    staged = sums.reshape(section_count, 2, 2, quarter, feature_width)
    kept = lax.dynamic_index_in_dim(staged, core_bit, 2, keepdims=False)
    sent = lax.dynamic_index_in_dim(staged, 1 - core_bit, 2, keepdims=False)
    packet = jnp.concatenate(
        [sent.reshape(section_count * half_rows, feature_width), local_weight_grad], axis=0
    )
    arrived = swap_with(packet, "rep", 1)
    kept = kept.reshape(section_count, half_rows, feature_width) + arrived[
        : section_count * half_rows
    ].reshape(section_count, half_rows, feature_width)
    weight_grad = team_scatter_sum(local_weight_grad + arrived[section_count * half_rows :])

    total = kept[reach_size]
    for s in range(section_count):
        if s != reach_size:
            moved = from_behind(kept[s].astype(jnp.bfloat16), "team", s - reach_size)
            total = total + moved.astype(jnp.float32)

    staged = total.reshape(2, quarter, feature_width)
    kept = lax.dynamic_index_in_dim(staged, chip_bit, 0, keepdims=False)
    sent = lax.dynamic_index_in_dim(staged, 1 - chip_bit, 0, keepdims=False)
    arrived = swap_with(jnp.concatenate([sent, weight_grad], axis=0), "rep", 2)
    gradient_share = (kept + arrived[:quarter]).astype(jnp.bfloat16)
    grad_weight = team_gather(weight_grad + arrived[quarter:]) * (1.0 / math.sqrt(nodes_total))
    return (activated, grad_weight, gradient_share)


def solution(mesh):
    placed = (
        P("team", None),
        P(),
        P(("team", "rep"), None),
        P(("team", "rep"), None, None, None, None),
        P(("team", "rep"), None, None),
        P(("team", "rep"), None),
    )

    return jax.shard_map(
        body,
        mesh=mesh,
        in_specs=placed,
        out_specs=(P(("team", "rep"), None), P(), P(("team", "rep"), None)),
        check_vma=False,
    )
```

```python
import functools
import math

import jax
import jax.numpy as jnp
from jax import lax
from jax.experimental import pallas as pl
from jax.experimental.pallas import tpu as pltpu
from jax.sharding import PartitionSpec as P


def from_behind(block, axis, distance):
    devices = range(lax.axis_size(axis))
    route = [((i - distance) % len(devices), i) for i in devices]
    return lax.ppermute(block, axis, route)


def butterfly_sum(block, axes):
    for axis in axes:
        size = lax.axis_size(axis)
        if size & (size - 1):
            block = lax.psum(block, axis)
            continue
        distance = 1
        while distance < size:
            route = [(i, i ^ distance) for i in range(size)]
            block = block + lax.ppermute(block, axis, route)
            distance *= 2
    return block


def layer_kernel(coords_ref, counts_ref, order_ref, *refs, section_count, slot_count, panel_dev, tile_size):
    feature_refs = refs[:section_count]
    tiles_ref, out_grad_ref, weight_ref, act_ref, wgrad_ref, sums_ref = refs[section_count:]
    weight = weight_ref[...]
    column_count = feature_refs[0].shape[0] // tile_size
    direct_first = slot_count == column_count

    def slot_entry(g, s, k):
        base = (g * section_count + s) * slot_count + k
        column = jnp.clip(coords_ref[base], 0, column_count - 1)
        live = k < counts_ref[g * section_count + s]
        return column, live

    aggregated_rows = []
    gate_rows = []
    for g in range(panel_dev):
        total = jnp.zeros((tile_size, weight.shape[1]), jnp.float32)
        for j in range(section_count):
            s = order_ref[j]
            for k in range(slot_count):
                column, live = slot_entry(g, s, k)
                start = pl.multiple_of(column * tile_size, tile_size)
                picked = feature_refs[j][pl.ds(start, tile_size), :]
                product = jnp.dot(tiles_ref[g, s, k], picked, preferred_element_type=jnp.float32)
                total = total + jnp.where(live, product, 0.0)
        aggregated = total.astype(jnp.bfloat16)
        pre_act = jnp.dot(aggregated, weight, preferred_element_type=jnp.float32)
        sigmoid_value = jax.nn.sigmoid(pre_act)
        rows = pl.ds(g * tile_size, tile_size)
        act_ref[rows, :] = (pre_act * sigmoid_value).astype(act_ref.dtype)
        out_grad = out_grad_ref[rows, :].astype(jnp.float32)
        gate = (out_grad * sigmoid_value * (1.0 + pre_act * (1.0 - sigmoid_value))).astype(jnp.bfloat16)
        aggregated_rows.append(aggregated)
        gate_rows.append(gate)

    aggregated_all = jnp.concatenate(aggregated_rows, axis=0)
    gate_all = jnp.concatenate(gate_rows, axis=0)
    wgrad_ref[...] = lax.dot_general(
        aggregated_all, gate_all, (((0,), (0,)), ((), ())), preferred_element_type=jnp.float32
    )
    if not direct_first:
        sums_ref[...] = jnp.zeros(sums_ref.shape, sums_ref.dtype)
    for g in range(panel_dev):
        back = lax.dot_general(
            gate_rows[g], weight, (((1,), (1,)), ((), ())), preferred_element_type=jnp.float32
        ).astype(jnp.bfloat16)
        for j in range(section_count):
            s = order_ref[j]
            for k in range(slot_count):
                column, live = slot_entry(g, s, k)
                start = pl.multiple_of(column * tile_size, tile_size)
                contrib = lax.dot_general(
                    tiles_ref[g, s, k], back, (((0,), (0,)), ((), ())),
                    preferred_element_type=jnp.float32,
                )
                contrib = jnp.where(live, contrib, 0.0)
                if g == 0 and direct_first:
                    sums_ref[s, pl.ds(start, tile_size), :] = contrib
                else:
                    sums_ref[s, pl.ds(start, tile_size), :] += contrib


def layer_call(source_blocks, order, tiles, out_grad, weight, coords, counts):
    panel_dev, section_count, slot_count, tile_size, _ = tiles.shape
    team_rows, feature_width = source_blocks[0].shape
    kernel = functools.partial(
        layer_kernel,
        section_count=section_count,
        slot_count=slot_count,
        panel_dev=panel_dev,
        tile_size=tile_size,
    )
    smem = pl.BlockSpec(memory_space=pltpu.SMEM)
    vmem = pl.BlockSpec(memory_space=pltpu.VMEM)
    matmuls = 2 * panel_dev * section_count * slot_count + 4 * panel_dev
    return pl.pallas_call(
        kernel,
        out_shape=(
            jax.ShapeDtypeStruct(out_grad.shape, jnp.bfloat16),
            jax.ShapeDtypeStruct((feature_width, feature_width), jnp.float32),
            jax.ShapeDtypeStruct((section_count, team_rows, feature_width), jnp.float32),
        ),
        in_specs=[smem, smem, smem] + [vmem] * (section_count + 3),
        out_specs=(vmem, vmem, vmem),
        compiler_params=pltpu.CompilerParams(vmem_limit_bytes=48 * 1024 * 1024),
        cost_estimate=pl.CostEstimate(
            flops=2 * matmuls * tile_size * tile_size * feature_width,
            transcendentals=panel_dev * tile_size * feature_width,
            bytes_accessed=tiles.size * 2 + section_count * team_rows * feature_width * 6,
        ),
    )(coords.reshape(-1), counts.reshape(-1), order, *source_blocks, tiles, out_grad, weight)


def swap_with(block, axis, mask):
    size = lax.axis_size(axis)
    route = [(i, i ^ mask) for i in range(size)]
    return lax.ppermute(block, axis, route)


def team_scatter_sum(block):
    size = lax.axis_size("team")
    rows = block.shape[0]
    pieces = lax.all_to_all(block.reshape(size, rows // size, -1), "team", 0, 0, tiled=True)
    return jnp.sum(pieces, axis=0)


def team_gather(piece):
    size = lax.axis_size("team")
    copies = jnp.broadcast_to(piece[None], (size,) + piece.shape)
    gathered = lax.all_to_all(copies, "team", 0, 0, tiled=True)
    return gathered.reshape(size * piece.shape[0], -1)


def gather_sources(features, reach_size, rep_size):
    team_size = lax.axis_size("team")
    if rep_size % 2:
        blocks = [features] + [
            from_behind(features, "team", -shift)
            for shift in range(-reach_size, reach_size + 1)
            if shift
        ]
        shifts = [0] + [shift for shift in range(-reach_size, reach_size + 1) if shift]
        order = jnp.array([reach_size + shift for shift in shifts], jnp.int32)
        return blocks, order
    sign = 1 - 2 * (lax.axis_index("rep") % 2)
    fetched = []
    for distance in range(1, reach_size + 1):
        route = []
        for team in range(team_size):
            for rep in range(rep_size):
                step = distance if rep % 2 == 0 else -distance
                source = ((team + step) % team_size) * rep_size + rep
                route.append((source, team * rep_size + rep))
        fetched.append(lax.ppermute(features, ("team", "rep"), route))
    swapped = swap_with(jnp.stack(fetched), "rep", 1)
    blocks = [features] + fetched + [swapped[i] for i in range(reach_size)]
    distances = jnp.arange(1, reach_size + 1, dtype=jnp.int32)
    order = jnp.concatenate(
        [jnp.array([reach_size], jnp.int32), reach_size + sign * distances, reach_size - sign * distances]
    ).astype(jnp.int32)
    return blocks, order


def body(features, weight, out_grad, tiles, coords, counts):
    _, section_count, _, _, _ = tiles.shape
    team_rows, feature_width = features.shape
    reach_size = (section_count - 1) // 2
    nodes_total = team_rows * lax.axis_size("team")
    rep_size = lax.axis_size("rep")
    source_blocks, order = gather_sources(features, reach_size, rep_size)
    activated, local_weight_grad, sums = layer_call(
        source_blocks, order, tiles, out_grad, weight, coords, counts
    )
    if rep_size != 4:
        grad_weight = butterfly_sum(local_weight_grad, ("rep", "team"))
        share = lax.psum_scatter(sums, "rep", scatter_dimension=1, tiled=True)
        total = share[reach_size]
        for s in range(section_count):
            if s != reach_size:
                arrived = from_behind(share[s].astype(jnp.bfloat16), "team", s - reach_size)
                total = total + arrived.astype(jnp.float32)
        return (activated, grad_weight * (1.0 / math.sqrt(nodes_total)), total.astype(jnp.bfloat16))

    rep_index = lax.axis_index("rep")
    core_bit = rep_index % 2
    chip_bit = rep_index // 2
    quarter = team_rows // 4
    half_rows = 2 * quarter
    staged = sums.reshape(section_count, 2, 2, quarter, feature_width)
    kept = lax.dynamic_index_in_dim(staged, core_bit, 2, keepdims=False)
    sent = lax.dynamic_index_in_dim(staged, 1 - core_bit, 2, keepdims=False)
    packet = jnp.concatenate(
        [sent.reshape(section_count * half_rows, feature_width), local_weight_grad], axis=0
    )
    arrived = swap_with(packet, "rep", 1)
    kept = kept.reshape(section_count, half_rows, feature_width) + arrived[
        : section_count * half_rows
    ].reshape(section_count, half_rows, feature_width)
    weight_grad = team_scatter_sum(local_weight_grad + arrived[section_count * half_rows :])
    weight_grad = team_gather(weight_grad)

    total = kept[reach_size]
    for s in sorted(range(section_count), key=lambda s: -abs(s - reach_size)):
        if s != reach_size:
            moved = from_behind(kept[s].astype(jnp.bfloat16), "team", s - reach_size)
            total = total + moved.astype(jnp.float32)

    staged = total.reshape(2, quarter, feature_width)
    kept = lax.dynamic_index_in_dim(staged, chip_bit, 0, keepdims=False)
    sent = lax.dynamic_index_in_dim(staged, 1 - chip_bit, 0, keepdims=False)
    arrived = swap_with(jnp.concatenate([sent, weight_grad], axis=0), "rep", 2)
    gradient_share = (kept + arrived[:quarter]).astype(jnp.bfloat16)
    grad_weight = (weight_grad + arrived[quarter:]) * (1.0 / math.sqrt(nodes_total))
    return (activated, grad_weight, gradient_share)


def solution(mesh):
    placed = (
        P("team", None),
        P(),
        P(("team", "rep"), None),
        P(("team", "rep"), None, None, None, None),
        P(("team", "rep"), None, None),
        P(("team", "rep"), None),
    )

    return jax.shard_map(
        body,
        mesh=mesh,
        in_specs=placed,
        out_specs=(P(("team", "rep"), None), P(), P(("team", "rep"), None)),
        check_vma=False,
    )
```
